512 devices in a mesh: pairs: 64 (over x, y, core), aux: 8 (over z).
Axes of the slice: x: 4, y: 8, z: 8, core: 2. Of those that a mesh axis runs over, the one named last changes fastest.
Arguments:
- amplitudes: bfloat16 [1024, 128, 128], P('pairs'), may hold values from -6 to 6
- pno_coef: bfloat16 [1024, 256, 128], P('pairs'), may hold values from -0.625 to 0.625
- ladder_ints: bfloat16 [320, 128, 128], P('aux'), may hold values from -0.3125 to 0.3125
- coulomb_ints: bfloat16 [1024, 128, 128], P(('pairs', 'aux')), may hold values from -6 to 6
- pno_energy: float32 [1024, 128], P(('pairs', 'aux')), may hold values from 0.3 to 3
- link_owner: int32 [49152, 1], P(('pairs', 'aux')), may hold values from 0 to 63; in each aligned block of 96 rows (0 to 95, 96 to 191, ...) at most 2 rows name the same one
- link_local: int32 [49152, 1], P(('pairs', 'aux')), may hold values from 0 to 15
Outputs:
- updated: float32 [1024, 128, 128], P(('pairs', 'aux'))
The draws below stay inside these ranges and needn't reach their ends.
Inputs may be any that keep to these rules, and one draw needn't show every extreme that they name: `link_owner`: in each device's aligned block of 96 rows no owner group is named by more than 2 rows, a bound that some block reaches.
All inputs are finite; a program needn't handle non-finite values.
Results may differ from the reference program's by a relative error of at most 0.0033.
Values may be sent and summed in bfloat16 or wider, within the bound.
No kernel may reach another device: no remote copies, remote signals or barrier semaphores. Data moves between devices by JAX's collectives and lax.ppermute only.
A program may use at most 128 MiB of HBM per device.

```python
import math
import jax
import jax.numpy as jnp
import numpy as np
from jax import lax

NPNO = 128
NPAO = 256
NAUXF = 320
PAIR_DEV = 16
LPS = 6
PAIRS = 1024
LINKS = 48
SLOTS = 96
CAP = 2
LINK_ROWS = 49152
N_PAIRS = 64
N_AUX = 8


def place_ends(values, rng, smallest, high):
    place = [jax.random.randint(jax.random.fold_in(rng, axis), (), 0, length) for axis, length in enumerate(values.shape)]
    longest = values.shape.index(max(values.shape))
    neighbour = place[:longest] + [(place[longest] + 1) % values.shape[longest]] + place[longest + 1:]
    return values.at[tuple(place)].set(smallest).at[tuple(neighbour)].set(high)


def level_of(stream_key, shape, shards, least, high):
    level, own = 1.0, jax.random.fold_in(stream_key, 6)
    for position, parts in shards:
        heights = jnp.exp(jax.random.uniform(jax.random.fold_in(own, position), (parts,), jnp.float32, least / len(shards), high / len(shards)))
        level = level * jnp.repeat(heights, shape[position] // parts).reshape([-1 if axis == position else 1 for axis in range(len(shape))])
    return level


def routed_block(rng, own, number, rows, amount, top, bound, skew):
    order = jax.random.permutation(rng, amount)
    heavy_load, ordinary = shares(amount, rows * top, bound, skew, True), shares(amount, rows * top, bound, skew, False)
    places = jnp.arange(amount)

    def named(lengths, turn):
        used = int((lengths > 0).sum())
        fixed = max(1, used // 4)
        moved = fixed + (places - fixed + turn * (used - fixed)) % max(1, amount - fixed)
        return jnp.zeros((amount,), jnp.int32).at[order[jnp.where(places < fixed, places, moved)]].set(jnp.asarray(lengths, jnp.int32))

    lengths = jnp.where(number % 4 == 0, named(heavy_load, number // 4), named(ordinary, number - number // 4 - 1))
    mixed = jax.random.permutation(jax.random.fold_in(own, 3), amount)
    source_of, sink = mixed[0:amount // 2 * 2:2], mixed[1:amount // 2 * 2:2]
    slack = jnp.minimum(lengths[source_of] - 1, bound - lengths[sink]) // 2
    slack = jnp.where((source_of == order[0]) | (sink == order[0]) | (lengths[sink] == 0), 0, jnp.maximum(slack, 0))
    moved = jax.random.randint(jax.random.fold_in(own, 4), (amount // 2,), 0, 1 << 20) % (slack + 1)
    lengths = lengths.at[source_of].add(-moved).at[sink].add(moved)
    members = jnp.searchsorted(jnp.cumsum(lengths), jnp.arange(rows * top), side="right").astype(jnp.int32)
    listing = members.reshape(top, rows).T
    listing = listing[jax.random.permutation(jax.random.fold_in(own, 1), rows)]
    turn = jax.random.randint(jax.random.fold_in(own, 2), (rows, 1), 0, top)
    return jnp.take_along_axis(listing, (jnp.arange(top)[None, :] + turn) % top, axis=1)


def shares(number_of, total, reach, skew, full):
    portions = [(1 << 20) // math.isqrt(grade ** skew) + 1 for grade in range(1, number_of + 1)]
    largest = reach if full else min(reach, max(-(-total // number_of), total * portions[0] // sum(portions)))
    least = 1 if total - largest >= number_of - 1 else 0
    given, rest = [largest] + [least] * (number_of - 1), total - largest - least * (number_of - 1)
    while rest > 0:
        candidates = [i for i in range(1, number_of) if given[i] < largest] or [i for i in range(1, number_of) if given[i] < reach]
        pool, left = sum([portions[i] for i in candidates]), rest
        for i in candidates:
            more = min(reach - given[i], max(1, left * portions[i] // pool), rest)
            given[i] = given[i] + more
            rest = rest - more
    return np.array(given)


def noise(own_key, dims, deviation, most, pieces=(), kind=jnp.bfloat16):
    level = level_of(own_key, dims, pieces, -0.22, 0.18) if pieces else 1.0
    values = jax.random.normal(own_key, dims, jnp.float32) * deviation * level
    return jnp.minimum(jnp.maximum(values, -most), most).astype(kind)


def setup_inputs(seed: int = 0) -> dict:
    splits = jax.random.split(jax.random.key(seed), 8)
    amplitudes = noise(splits[0], (PAIRS, NPNO, NPNO), 1.0, 6.0, ((0, 64),))
    pno_coef = noise(splits[1], (PAIRS, NPAO, NPNO), ((LINKS * NPNO * NPNO) ** -0.125 * NPAO ** -0.25), 0.625, ((0, 64),))
    ladder_ints = noise(splits[2], (NAUXF, NPNO, NPNO), ((NAUXF * NPNO * NPNO) ** -0.25), 0.3125, ((0, 8),))
    coulomb_ints = noise(splits[3], (PAIRS, NPNO, NPNO), 1.0, 6.0, ((0, 512),))
    pno_energy = jnp.clip(jnp.exp(math.log(3.0) - 2.3025851 * jax.random.uniform(splits[4], (PAIRS, NPNO), jnp.float32) ** level_of(splits[4], (PAIRS, NPNO), ((0, 512),), -0.2, 0.2)), 0.3, 3.0)
    link_owner_keys = jax.random.split(jax.random.fold_in(splits[5], 1), LINK_ROWS // SLOTS)
    link_owner_turns = jax.random.permutation(jax.random.fold_in(splits[5], 3), LINK_ROWS // SLOTS)
    link_owner = jax.vmap(lambda own, number: routed_block(jax.random.fold_in(splits[5], 2), own, number, SLOTS, N_PAIRS, 1, CAP, 2))(link_owner_keys, link_owner_turns).reshape((LINK_ROWS, 1))
    link_local = place_ends(jax.random.randint(splits[6], (LINK_ROWS, 1), 0, PAIR_DEV), jax.random.fold_in(splits[6], 1), 0, PAIR_DEV - 1).astype(jnp.int32)
    return {"amplitudes": amplitudes, "pno_coef": pno_coef, "ladder_ints": ladder_ints, "coulomb_ints": coulomb_ints, "pno_energy": pno_energy, "link_owner": link_owner, "link_local": link_local}


def reference(amplitudes, pno_coef, ladder_ints, coulomb_ints, pno_energy, link_owner, link_local):
    target = (link_owner[:, 0] * PAIR_DEV + link_local[:, 0]).astype(jnp.int32)
    target = jnp.transpose(target.reshape(N_PAIRS, N_AUX, PAIR_DEV, LPS), (0, 2, 1, 3)).reshape(PAIRS, LINKS)
    blocks = ladder_ints.astype(jnp.float32)

    def one_pair(inputs):
        coef_p, amp_p, targets = inputs
        coef_q = pno_coef[targets].astype(jnp.float32)
        amp_q = amplitudes[targets].astype(jnp.float32)
        intersection = jnp.einsum("ac,lad->lcd", coef_p.astype(jnp.float32), coef_q).astype(jnp.bfloat16)
        intersection = lax.optimization_barrier(intersection).astype(jnp.float32)
        halfway = jnp.einsum("lcd,lde->lce", intersection, amp_q).astype(jnp.bfloat16)
        halfway = lax.optimization_barrier(halfway).astype(jnp.float32)
        linked = jnp.einsum("lce,lfe->cf", halfway, intersection)
        ladder_half = jnp.einsum("qcd,de->qce", blocks, amp_p.astype(jnp.float32)).astype(jnp.bfloat16)
        ladder_half = lax.optimization_barrier(ladder_half).astype(jnp.float32)
        ladder = jnp.einsum("qce,qfe->cf", ladder_half, blocks)
        return linked + ladder

    pair_sums = lax.map(one_pair, (pno_coef, amplitudes, target))
    residual = coulomb_ints.astype(jnp.float32) + pair_sums
    denominator = pno_energy[:, :, None] + pno_energy[:, None, :]
    return amplitudes.astype(jnp.float32) - residual / denominator
```

```python
import jax
import jax.numpy as jnp
from jax import lax
from jax.sharding import PartitionSpec as P


def local(amplitudes, pno_coef, ladder_ints, coulomb_ints, pno_energy, link_owner, link_local):
    groups = lax.axis_size("pairs")
    pair_dev = amplitudes.shape[0]
    own_rows = coulomb_ints.shape[0]
    slot_count = link_owner.shape[0]
    per_slice = slot_count // pair_dev
    capacity = max(2, (5 * slot_count + 4 * groups - 1) // (4 * groups))
    pno_width = amplitudes.shape[1]
    pao_width = pno_coef.shape[1]
    owner_group = link_owner[:, 0]
    local_index = link_local[:, 0]
    slot_order = jnp.arange(slot_count, dtype=jnp.int32)
    same_owner = (owner_group[:, None] == owner_group[None, :]) & (
        slot_order[None, :] < slot_order[:, None]
    )
    slot_rank = jnp.sum(same_owner.astype(jnp.int32), axis=1)
    bucket = owner_group * capacity + slot_rank
    places = jnp.arange(groups * capacity, dtype=jnp.int32)
    match_table = (bucket[:, None] == places[None, :]).astype(jnp.int32)
    wanted = jnp.sum(match_table * (local_index[:, None] + 1), axis=0) - 1
    asked_rows = lax.all_to_all(
        wanted.reshape(groups, capacity), "pairs", split_axis=0, concat_axis=0, tiled=True
    )
    picked = jnp.maximum(asked_rows, 0)
    amp_items = amplitudes[picked]
    coef_items = pno_coef[picked]
    got_coef = lax.all_to_all(coef_items, "pairs", split_axis=0, concat_axis=0, tiled=True)
    got_amp = lax.all_to_all(amp_items, "pairs", split_axis=0, concat_axis=0, tiled=True)
    flat_amp = got_amp.reshape(groups * capacity, pno_width, pno_width)
    flat_coef = got_coef.reshape(groups * capacity, pao_width, pno_width)

    ladder_half = jnp.einsum(
        "qcd,pde->pqce", ladder_ints, amplitudes, preferred_element_type=jnp.float32
    ).astype(jnp.bfloat16)
    ladder = jnp.einsum(
        "pqce,qfe->pcf", ladder_half, ladder_ints, preferred_element_type=jnp.float32
    )
    ladder = lax.optimization_barrier(ladder)

    coef_q = flat_coef[bucket].reshape(pair_dev, per_slice, pao_width, pno_width)
    amp_q = flat_amp[bucket].reshape(pair_dev, per_slice, pno_width, pno_width)
    intersection = jnp.einsum(
        "pac,plad->plcd", pno_coef, coef_q, preferred_element_type=jnp.float32
    ).astype(jnp.bfloat16)
    halfway = jnp.einsum(
        "plcd,plde->plce", intersection, amp_q, preferred_element_type=jnp.float32
    ).astype(jnp.bfloat16)
    linked = jnp.einsum(
        "plce,plfe->pcf", halfway, intersection, preferred_element_type=jnp.float32
    )

    partial_value = linked + ladder
    reduced = lax.psum_scatter(partial_value, "aux", scatter_dimension=0, tiled=True)
    first_row = lax.axis_index("aux") * own_rows
    amp_mine = lax.dynamic_slice_in_dim(amplitudes, first_row, own_rows, 0)
    residual = coulomb_ints.astype(jnp.float32) + reduced
    denominator = pno_energy[:, :, None] + pno_energy[:, None, :]
    return amp_mine.astype(jnp.float32) - residual / denominator


def solution(mesh):
    in_specs = (
        P("pairs", None, None),
        P("pairs", None, None),
        P("aux", None, None),
        P(("pairs", "aux"), None, None),
        P(("pairs", "aux"), None),
        P(("pairs", "aux"), None),
        P(("pairs", "aux"), None),
    )
    out_specs = P(("pairs", "aux"), None, None)
    return jax.shard_map(local, mesh=mesh, in_specs=in_specs, out_specs=out_specs, check_vma=False)
```

```python
import jax
import jax.numpy as jnp
from jax import lax
from jax.sharding import PartitionSpec as P


def local(amplitudes, pno_coef, ladder_ints, coulomb_ints, pno_energy, link_owner, link_local):
    groups = lax.axis_size("pairs")
    pair_dev = amplitudes.shape[0]
    own_rows = coulomb_ints.shape[0]
    slot_count = link_owner.shape[0]
    per_slice = slot_count // pair_dev
    capacity = max(2, (5 * slot_count + 4 * groups - 1) // (4 * groups))
    pno_width = amplitudes.shape[1]
    pao_width = pno_coef.shape[1]
    owner_group = link_owner[:, 0]
    local_index = link_local[:, 0]
    slot_order = jnp.arange(slot_count, dtype=jnp.int32)
    same_owner = (owner_group[:, None] == owner_group[None, :]) & (
        slot_order[None, :] < slot_order[:, None]
    )
    slot_rank = jnp.sum(same_owner.astype(jnp.int32), axis=1)
    bucket = owner_group * capacity + slot_rank
    places = jnp.arange(groups * capacity, dtype=jnp.int32)
    match_table = (bucket[:, None] == places[None, :]).astype(jnp.int32)
    wanted = jnp.sum(match_table * (local_index[:, None] + 1), axis=0) - 1
    asked_rows = lax.all_to_all(
        wanted.reshape(groups, capacity), "pairs", split_axis=0, concat_axis=0, tiled=True
    )
    picked = jnp.maximum(asked_rows, 0)
    both = jnp.concatenate([pno_coef, amplitudes], axis=1)
    items = both[picked.reshape(groups * capacity)]
    flat = lax.all_to_all(items, "pairs", split_axis=0, concat_axis=0, tiled=True)

    ladder_half = jnp.einsum(
        "qcd,pde->pqce", ladder_ints, amplitudes, preferred_element_type=jnp.float32
    ).astype(jnp.bfloat16)
    ladder = jnp.einsum(
        "pqce,qfe->pcf", ladder_half, ladder_ints, preferred_element_type=jnp.float32
    )
    ladder = lax.optimization_barrier(ladder)

    rows = flat[bucket]
    coef_q = rows[:, :pao_width].reshape(pair_dev, per_slice, pao_width, pno_width)
    amp_q = rows[:, pao_width:].reshape(pair_dev, per_slice, pno_width, pno_width)
    intersection = jnp.einsum(
        "pac,plad->plcd", pno_coef, coef_q, preferred_element_type=jnp.float32
    ).astype(jnp.bfloat16)
    halfway = jnp.einsum(
        "plcd,plde->plce", intersection, amp_q, preferred_element_type=jnp.float32
    ).astype(jnp.bfloat16)
    linked = jnp.einsum(
        "plce,plfe->pcf", halfway, intersection, preferred_element_type=jnp.float32
    )

    partial_value = linked + ladder
    aux_count = lax.axis_size("aux")
    pieces = partial_value.reshape(aux_count, own_rows, pno_width, pno_width)
    reduced = jnp.sum(
        lax.all_to_all(pieces, "aux", split_axis=0, concat_axis=0, tiled=True), axis=0
    )
    first_row = lax.axis_index("aux") * own_rows
    amp_mine = lax.dynamic_slice_in_dim(amplitudes, first_row, own_rows, 0)
    residual = coulomb_ints.astype(jnp.float32) + reduced
    denominator = pno_energy[:, :, None] + pno_energy[:, None, :]
    return amp_mine.astype(jnp.float32) - residual / denominator


def solution(mesh):
    in_specs = (
        P("pairs", None, None),
        P("pairs", None, None),
        P("aux", None, None),
        P(("pairs", "aux"), None, None),
        P(("pairs", "aux"), None),
        P(("pairs", "aux"), None),
        P(("pairs", "aux"), None),
    )
    out_specs = P(("pairs", "aux"), None, None)
    return jax.shard_map(local, mesh=mesh, in_specs=in_specs, out_specs=out_specs, check_vma=False)
```

```python
import jax
import jax.numpy as jnp
from jax import lax
from jax.sharding import PartitionSpec as P


def local(amplitudes, pno_coef, ladder_ints, coulomb_ints, pno_energy, link_owner, link_local):
    groups = lax.axis_size("pairs")
    pair_dev = amplitudes.shape[0]
    own_rows = coulomb_ints.shape[0]
    slot_count = link_owner.shape[0]
    per_slice = slot_count // pair_dev
    capacity = max(2, (5 * slot_count + 4 * groups - 1) // (4 * groups))
    pno_width = amplitudes.shape[1]
    pao_width = pno_coef.shape[1]
    owner_group = link_owner[:, 0]
    local_index = link_local[:, 0]
    slot_order = jnp.arange(slot_count, dtype=jnp.int32)
    same_owner = (owner_group[:, None] == owner_group[None, :]) & (
        slot_order[None, :] < slot_order[:, None]
    )
    slot_rank = jnp.sum(same_owner.astype(jnp.int32), axis=1)
    bucket = owner_group * capacity + slot_rank
    places = jnp.arange(groups * capacity, dtype=jnp.int32)
    match_table = (bucket[:, None] == places[None, :]).astype(jnp.int32)
    wanted = jnp.sum(match_table * (local_index[:, None] + 1), axis=0) - 1
    asked_rows = lax.all_to_all(
        wanted.reshape(groups, capacity), "pairs", split_axis=0, concat_axis=0, tiled=True
    )
    picked = jnp.maximum(asked_rows, 0)
    both = jnp.concatenate([pno_coef, amplitudes], axis=1)
    items = both[picked.reshape(groups * capacity)]
    flat = lax.all_to_all(items, "pairs", split_axis=0, concat_axis=0, tiled=True)

    ladder_half = jnp.einsum(
        "qcd,pde->pqce", ladder_ints, amplitudes, preferred_element_type=jnp.float32
    ).astype(jnp.bfloat16)
    ladder = jnp.einsum(
        "pqce,qfe->pcf", ladder_half, ladder_ints, preferred_element_type=jnp.float32
    )
    ladder_mine = lax.psum_scatter(ladder, "aux", scatter_dimension=0, tiled=True)

    rows = flat[bucket]
    coef_q = rows[:, :pao_width].reshape(pair_dev, per_slice, pao_width, pno_width)
    amp_q = rows[:, pao_width:].reshape(pair_dev, per_slice, pno_width, pno_width)
    intersection = jnp.einsum(
        "pac,plad->plcd", pno_coef, coef_q, preferred_element_type=jnp.float32
    ).astype(jnp.bfloat16)
    halfway = jnp.einsum(
        "plcd,plde->plce", intersection, amp_q, preferred_element_type=jnp.float32
    ).astype(jnp.bfloat16)
    linked = jnp.einsum(
        "plce,plfe->pcf", halfway, intersection, preferred_element_type=jnp.float32
    )

    aux_count = lax.axis_size("aux")
    pieces = linked.astype(jnp.bfloat16).reshape(aux_count, own_rows, pno_width, pno_width)
    linked_mine = jnp.sum(
        lax.all_to_all(pieces, "aux", split_axis=0, concat_axis=0, tiled=True).astype(jnp.float32),
        axis=0,
    )
    reduced = ladder_mine + linked_mine
    first_row = lax.axis_index("aux") * own_rows
    amp_mine = lax.dynamic_slice_in_dim(amplitudes, first_row, own_rows, 0)
    residual = coulomb_ints.astype(jnp.float32) + reduced
    denominator = pno_energy[:, :, None] + pno_energy[:, None, :]
    return amp_mine.astype(jnp.float32) - residual / denominator


def solution(mesh):
    in_specs = (
        P("pairs", None, None),
        P("pairs", None, None),
        P("aux", None, None),
        P(("pairs", "aux"), None, None),
        P(("pairs", "aux"), None),
        P(("pairs", "aux"), None),
        P(("pairs", "aux"), None),
    )
    out_specs = P(("pairs", "aux"), None, None)
    return jax.shard_map(local, mesh=mesh, in_specs=in_specs, out_specs=out_specs, check_vma=False)
```

```python
import jax
import jax.numpy as jnp
from jax import lax
from jax.experimental import pallas as pl
from jax.experimental.pallas import tpu as pltpu
from jax.sharding import PartitionSpec as P


def linked_kernel(links, pao_width, bucket_ref, coef_t_ref, *refs):
    slot_refs, out_ref = refs[:links], refs[links]
    coef_t = coef_t_ref[0]
    total = None
    for slot_ref in slot_refs:
        coef_q = slot_ref[0, :pao_width, :]
        amp_q = slot_ref[0, pao_width:, :]
        overlap = jnp.dot(coef_t, coef_q, preferred_element_type=jnp.float32).astype(jnp.bfloat16)
        half = jnp.dot(overlap, amp_q, preferred_element_type=jnp.float32).astype(jnp.bfloat16)
        term = lax.dot_general(
            half, overlap, (((1,), (1,)), ((), ())), preferred_element_type=jnp.float32
        )
        total = term if total is None else total + term
    out_ref[0] = total.astype(out_ref.dtype)


def linked_sum(bucket, coef_t, flat, links):
    pair_dev, pno_width, pao_width = coef_t.shape
    row_width = flat.shape[1]

    def slot_spec(j):
        return pl.BlockSpec((1, row_width, pno_width), lambda p, b: (b[p * links + j], 0, 0))

    grid_spec = pltpu.PrefetchScalarGridSpec(
        num_scalar_prefetch=1,
        grid=(pair_dev,),
        in_specs=[pl.BlockSpec((1, pno_width, pao_width), lambda p, b: (p, 0, 0))]
        + [slot_spec(j) for j in range(links)],
        out_specs=pl.BlockSpec((1, pno_width, pno_width), lambda p, b: (p, 0, 0)),
    )
    flops = pair_dev * links * 2 * pno_width * pno_width * (pao_width + 2 * pno_width)
    return pl.pallas_call(
        lambda *r: linked_kernel(links, pao_width, *r),
        grid_spec=grid_spec,
        out_shape=jax.ShapeDtypeStruct((pair_dev, pno_width, pno_width), jnp.bfloat16),
        cost_estimate=pl.CostEstimate(
            flops=flops,
            bytes_accessed=pair_dev * (links * row_width + pao_width + pno_width) * pno_width * 2,
            transcendentals=0,
        ),
    )(bucket, coef_t, *([flat] * links))


def local(amplitudes, pno_coef, ladder_ints, coulomb_ints, pno_energy, link_owner, link_local):
    groups = lax.axis_size("pairs")
    pair_dev = amplitudes.shape[0]
    own_rows = coulomb_ints.shape[0]
    slot_count = link_owner.shape[0]
    per_slice = slot_count // pair_dev
    capacity = max(2, (5 * slot_count + 4 * groups - 1) // (4 * groups))
    pno_width = amplitudes.shape[1]
    pao_width = pno_coef.shape[1]
    owner_group = link_owner[:, 0]
    local_index = link_local[:, 0]
    slot_order = jnp.arange(slot_count, dtype=jnp.int32)
    same_owner = (owner_group[:, None] == owner_group[None, :]) & (
        slot_order[None, :] < slot_order[:, None]
    )
    slot_rank = jnp.sum(same_owner.astype(jnp.int32), axis=1)
    bucket = owner_group * capacity + slot_rank
    places = jnp.arange(groups * capacity, dtype=jnp.int32)
    match_table = (bucket[:, None] == places[None, :]).astype(jnp.int32)
    wanted = jnp.sum(match_table * (local_index[:, None] + 1), axis=0) - 1
    asked_rows = lax.all_to_all(
        wanted.reshape(groups, capacity), "pairs", split_axis=0, concat_axis=0, tiled=True
    )
    picked = jnp.maximum(asked_rows, 0)
    both = jnp.concatenate([pno_coef, amplitudes], axis=1)
    items = both[picked.reshape(groups * capacity)]
    flat = lax.all_to_all(items, "pairs", split_axis=0, concat_axis=0, tiled=True)

    ladder_half = jnp.einsum(
        "qcd,pde->pqce", ladder_ints, amplitudes, preferred_element_type=jnp.float32
    ).astype(jnp.bfloat16)
    ladder = jnp.einsum(
        "pqce,qfe->pcf", ladder_half, ladder_ints, preferred_element_type=jnp.float32
    )
    ladder_mine = lax.psum_scatter(ladder, "aux", scatter_dimension=0, tiled=True)

    coef_t = jnp.transpose(pno_coef, (0, 2, 1))
    linked = linked_sum(bucket, coef_t, flat, per_slice)

    aux_count = lax.axis_size("aux")
    pieces = linked.reshape(aux_count, own_rows, pno_width, pno_width)
    linked_mine = jnp.sum(
        lax.all_to_all(pieces, "aux", split_axis=0, concat_axis=0, tiled=True).astype(jnp.float32),
        axis=0,
    )
    reduced = ladder_mine + linked_mine
    first_row = lax.axis_index("aux") * own_rows
    amp_mine = lax.dynamic_slice_in_dim(amplitudes, first_row, own_rows, 0)
    residual = coulomb_ints.astype(jnp.float32) + reduced
    denominator = pno_energy[:, :, None] + pno_energy[:, None, :]
    return amp_mine.astype(jnp.float32) - residual / denominator


def solution(mesh):
    in_specs = (
        P("pairs", None, None),
        P("pairs", None, None),
        P("aux", None, None),
        P(("pairs", "aux"), None, None),
        P(("pairs", "aux"), None),
        P(("pairs", "aux"), None),
        P(("pairs", "aux"), None),
    )
    out_specs = P(("pairs", "aux"), None, None)
    return jax.shard_map(local, mesh=mesh, in_specs=in_specs, out_specs=out_specs, check_vma=False)
```

```python
import jax
import jax.numpy as jnp
from jax import lax
from jax.experimental import pallas as pl
from jax.experimental.pallas import tpu as pltpu
from jax.sharding import PartitionSpec as P


def linked_kernel(links, pao_width, bucket_ref, coef_t_ref, *refs):
    slot_refs, out_ref = refs[:links], refs[links]
    coef_t = coef_t_ref[0]
    total = None
    for slot_ref in slot_refs:
        coef_q = slot_ref[0, :pao_width, :]
        amp_q = slot_ref[0, pao_width:, :]
        overlap = jnp.dot(coef_t, coef_q, preferred_element_type=jnp.float32).astype(jnp.bfloat16)
        half = jnp.dot(overlap, amp_q, preferred_element_type=jnp.float32).astype(jnp.bfloat16)
        term = lax.dot_general(
            half, overlap, (((1,), (1,)), ((), ())), preferred_element_type=jnp.float32
        )
        total = term if total is None else total + term
    out_ref[0] = total.astype(out_ref.dtype)


def linked_sum(bucket, coef_t, flat, links):
    pair_dev, pno_width, pao_width = coef_t.shape
    row_width = flat.shape[1]

    def slot_spec(j):
        return pl.BlockSpec((1, row_width, pno_width), lambda p, b: (b[p * links + j], 0, 0))

    grid_spec = pltpu.PrefetchScalarGridSpec(
        num_scalar_prefetch=1,
        grid=(pair_dev,),
        in_specs=[pl.BlockSpec((1, pno_width, pao_width), lambda p, b: (p, 0, 0))]
        + [slot_spec(j) for j in range(links)],
        out_specs=pl.BlockSpec((1, pno_width, pno_width), lambda p, b: (p, 0, 0)),
    )
    flops = pair_dev * links * 2 * pno_width * pno_width * (pao_width + 2 * pno_width)
    return pl.pallas_call(
        lambda *r: linked_kernel(links, pao_width, *r),
        grid_spec=grid_spec,
        out_shape=jax.ShapeDtypeStruct((pair_dev, pno_width, pno_width), jnp.bfloat16),
        cost_estimate=pl.CostEstimate(
            flops=flops,
            bytes_accessed=pair_dev * (links * row_width + pao_width + pno_width) * pno_width * 2,
            transcendentals=0,
        ),
    )(bucket, coef_t, *([flat] * links))


def local(amplitudes, pno_coef, ladder_ints, coulomb_ints, pno_energy, link_owner, link_local):
    groups = lax.axis_size("pairs")
    pair_dev = amplitudes.shape[0]
    own_rows = coulomb_ints.shape[0]
    slot_count = link_owner.shape[0]
    per_slice = slot_count // pair_dev
    capacity = max(2, (5 * slot_count + 4 * groups - 1) // (4 * groups))
    pno_width = amplitudes.shape[1]
    pao_width = pno_coef.shape[1]
    owner_group = link_owner[:, 0]
    local_index = link_local[:, 0]
    slot_order = jnp.arange(slot_count, dtype=jnp.int32)
    same_owner = (owner_group[:, None] == owner_group[None, :]) & (
        slot_order[None, :] < slot_order[:, None]
    )
    slot_rank = jnp.sum(same_owner.astype(jnp.int32), axis=1)
    bucket = owner_group * capacity + slot_rank
    places = jnp.arange(groups * capacity, dtype=jnp.int32)
    match_table = (bucket[:, None] == places[None, :]).astype(jnp.int32)
    wanted = jnp.sum(match_table * (local_index[:, None] + 1), axis=0) - 1
    asked_rows = lax.all_to_all(
        wanted.reshape(groups, capacity), "pairs", split_axis=0, concat_axis=0, tiled=True
    )
    picked = jnp.maximum(asked_rows, 0)
    both = jnp.concatenate([pno_coef, amplitudes], axis=1)
    items = both[picked.reshape(groups * capacity)]
    flat = lax.all_to_all(items, "pairs", split_axis=0, concat_axis=0, tiled=True)

    ladder_half = jnp.einsum(
        "qcd,pde->pqce", ladder_ints, amplitudes, preferred_element_type=jnp.float32
    ).astype(jnp.bfloat16)
    ladder = jnp.einsum(
        "pqce,qfe->pcf", ladder_half, ladder_ints, preferred_element_type=jnp.float32
    )
    aux_count = lax.axis_size("aux")
    aux_me = lax.axis_index("aux")
    ladder_mine = lax.dynamic_slice_in_dim(ladder, aux_me * own_rows, own_rows, 0)
    for shift in range(1, aux_count):
        goes_to = lax.rem(aux_me + shift, aux_count)
        piece = lax.dynamic_slice_in_dim(ladder, goes_to * own_rows, own_rows, 0)
        ladder_mine = ladder_mine + lax.ppermute(
            piece, "aux", [(i, (i + shift) % aux_count) for i in range(aux_count)]
        )

    flat, ladder_mine = lax.optimization_barrier((flat, ladder_mine))

    coef_t = jnp.transpose(pno_coef, (0, 2, 1))
    linked = linked_sum(bucket, coef_t, flat, per_slice)

    pieces = linked.reshape(aux_count, own_rows, pno_width, pno_width)
    linked_mine = jnp.sum(
        lax.all_to_all(pieces, "aux", split_axis=0, concat_axis=0, tiled=True).astype(jnp.float32),
        axis=0,
    )
    reduced = ladder_mine + linked_mine
    first_row = lax.axis_index("aux") * own_rows
    amp_mine = lax.dynamic_slice_in_dim(amplitudes, first_row, own_rows, 0)
    residual = coulomb_ints.astype(jnp.float32) + reduced
    denominator = pno_energy[:, :, None] + pno_energy[:, None, :]
    return amp_mine.astype(jnp.float32) - residual / denominator


def solution(mesh):
    in_specs = (
        P("pairs", None, None),
        P("pairs", None, None),
        P("aux", None, None),
        P(("pairs", "aux"), None, None),
        P(("pairs", "aux"), None),
        P(("pairs", "aux"), None),
        P(("pairs", "aux"), None),
    )
    out_specs = P(("pairs", "aux"), None, None)
    return jax.shard_map(local, mesh=mesh, in_specs=in_specs, out_specs=out_specs, check_vma=False)
```

```python
import jax
import jax.numpy as jnp
from jax import lax
from jax.experimental import pallas as pl
from jax.experimental.pallas import tpu as pltpu
from jax.sharding import PartitionSpec as P


def linked_kernel(links, pao_width, bucket_ref, coef_t_ref, *refs):
    slot_refs, out_ref = refs[:-1], refs[-1]
    pno_width = out_ref.shape[-1]
    for i in range(out_ref.shape[0]):
        mine = slot_refs[i * links:(i + 1) * links]
        coef_q = jnp.concatenate([r[0, :pao_width, :] for r in mine], axis=1)
        overlap = jnp.dot(coef_t_ref[i], coef_q, preferred_element_type=jnp.float32).astype(
            jnp.bfloat16
        )
        half = jnp.concatenate(
            [
                jnp.dot(
                    overlap[:, j * pno_width:(j + 1) * pno_width],
                    r[0, pao_width:, :],
                    preferred_element_type=jnp.float32,
                ).astype(jnp.bfloat16)
                for j, r in enumerate(mine)
            ],
            axis=1,
        )
        total = lax.dot_general(
            half, overlap, (((1,), (1,)), ((), ())), preferred_element_type=jnp.float32
        )
        out_ref[i] = total.astype(out_ref.dtype)


def linked_sum(bucket, coef_t, flat, links, step_pairs=4):
    pair_dev, pno_width, pao_width = coef_t.shape
    row_width = flat.shape[1]
    step_slots = step_pairs * links

    def slot_spec(j):
        return pl.BlockSpec(
            (1, row_width, pno_width), lambda p, b: (b[p * step_slots + j], 0, 0)
        )

    grid_spec = pltpu.PrefetchScalarGridSpec(
        num_scalar_prefetch=1,
        grid=(pair_dev // step_pairs,),
        in_specs=[pl.BlockSpec((step_pairs, pno_width, pao_width), lambda p, b: (p, 0, 0))]
        + [slot_spec(j) for j in range(step_slots)],
        out_specs=pl.BlockSpec((step_pairs, pno_width, pno_width), lambda p, b: (p, 0, 0)),
    )
    flops = pair_dev * links * 2 * pno_width * pno_width * (pao_width + 2 * pno_width)
    return pl.pallas_call(
        lambda *r: linked_kernel(links, pao_width, *r),
        grid_spec=grid_spec,
        out_shape=jax.ShapeDtypeStruct((pair_dev, pno_width, pno_width), jnp.bfloat16),
        cost_estimate=pl.CostEstimate(
            flops=flops,
            bytes_accessed=pair_dev * (links * row_width + pao_width + pno_width) * pno_width * 2,
            transcendentals=0,
        ),
    )(bucket, coef_t, *([flat] * step_slots))


def local(amplitudes, pno_coef, ladder_ints, coulomb_ints, pno_energy, link_owner, link_local):
    groups = lax.axis_size("pairs")
    pair_dev = amplitudes.shape[0]
    own_rows = coulomb_ints.shape[0]
    slot_count = link_owner.shape[0]
    per_slice = slot_count // pair_dev
    capacity = max(2, (5 * slot_count + 4 * groups - 1) // (4 * groups))
    pno_width = amplitudes.shape[1]
    pao_width = pno_coef.shape[1]
    owner_group = link_owner[:, 0]
    local_index = link_local[:, 0]
    slot_order = jnp.arange(slot_count, dtype=jnp.int32)
    same_owner = (owner_group[:, None] == owner_group[None, :]) & (
        slot_order[None, :] < slot_order[:, None]
    )
    slot_rank = jnp.sum(same_owner.astype(jnp.int32), axis=1)
    bucket = owner_group * capacity + slot_rank
    places = jnp.arange(groups * capacity, dtype=jnp.int32)
    match_table = (bucket[:, None] == places[None, :]).astype(jnp.int32)
    wanted = jnp.sum(match_table * (local_index[:, None] + 1), axis=0) - 1
    asked_rows = lax.all_to_all(
        wanted.reshape(groups, capacity), "pairs", split_axis=0, concat_axis=0, tiled=True
    )
    picked = jnp.maximum(asked_rows, 0)
    both = jnp.concatenate([pno_coef, amplitudes], axis=1)
    items = both[picked.reshape(groups * capacity)]
    flat = lax.all_to_all(items, "pairs", split_axis=0, concat_axis=0, tiled=True)

    ladder_half = jnp.einsum(
        "qcd,pde->pqce", ladder_ints, amplitudes, preferred_element_type=jnp.float32
    ).astype(jnp.bfloat16)
    ladder = jnp.einsum(
        "pqce,qfe->pcf", ladder_half, ladder_ints, preferred_element_type=jnp.float32
    )
    aux_count = lax.axis_size("aux")
    aux_me = lax.axis_index("aux")
    ladder_mine = lax.dynamic_slice_in_dim(ladder, aux_me * own_rows, own_rows, 0)
    for shift in range(1, aux_count):
        goes_to = lax.rem(aux_me + shift, aux_count)
        piece = lax.dynamic_slice_in_dim(ladder, goes_to * own_rows, own_rows, 0)
        ladder_mine = ladder_mine + lax.ppermute(
            piece, "aux", [(i, (i + shift) % aux_count) for i in range(aux_count)]
        )

    flat, ladder_mine = lax.optimization_barrier((flat, ladder_mine))

    coef_t = jnp.transpose(pno_coef, (0, 2, 1))
    linked = linked_sum(bucket, coef_t, flat, per_slice)

    pieces = linked.reshape(aux_count, own_rows, pno_width, pno_width)
    linked_mine = jnp.sum(
        lax.all_to_all(pieces, "aux", split_axis=0, concat_axis=0, tiled=True).astype(jnp.float32),
        axis=0,
    )
    reduced = ladder_mine + linked_mine
    first_row = lax.axis_index("aux") * own_rows
    amp_mine = lax.dynamic_slice_in_dim(amplitudes, first_row, own_rows, 0)
    residual = coulomb_ints.astype(jnp.float32) + reduced
    denominator = pno_energy[:, :, None] + pno_energy[:, None, :]
    return amp_mine.astype(jnp.float32) - residual / denominator


def solution(mesh):
    in_specs = (
        P("pairs", None, None),
        P("pairs", None, None),
        P("aux", None, None),
        P(("pairs", "aux"), None, None),
        P(("pairs", "aux"), None),
        P(("pairs", "aux"), None),
        P(("pairs", "aux"), None),
    )
    out_specs = P(("pairs", "aux"), None, None)
    return jax.shard_map(local, mesh=mesh, in_specs=in_specs, out_specs=out_specs, check_vma=False)
```

```python
import jax
import jax.numpy as jnp
from jax import lax
from jax.experimental import pallas as pl
from jax.experimental.pallas import tpu as pltpu
from jax.sharding import PartitionSpec as P


def linked_kernel(links, pao_width, bucket_ref, coef_t_ref, *refs):
    slot_refs, out_ref = refs[:-1], refs[-1]
    pno_width = out_ref.shape[-1]
    for i in range(out_ref.shape[0]):
        mine = slot_refs[i * links:(i + 1) * links]
        coef_q = jnp.concatenate([r[0, :pao_width, :] for r in mine], axis=1)
        overlap = jnp.dot(coef_t_ref[i], coef_q, preferred_element_type=jnp.float32).astype(
            jnp.bfloat16
        )
        half = jnp.concatenate(
            [
                jnp.dot(
                    overlap[:, j * pno_width:(j + 1) * pno_width],
                    r[0, pao_width:, :],
                    preferred_element_type=jnp.float32,
                ).astype(jnp.bfloat16)
                for j, r in enumerate(mine)
            ],
            axis=1,
        )
        total = lax.dot_general(
            half, overlap, (((1,), (1,)), ((), ())), preferred_element_type=jnp.float32
        )
        out_ref[i] = total.astype(out_ref.dtype)


def linked_sum(bucket, coef_t, flat, links, step_pairs=4):
    pair_dev, pno_width, pao_width = coef_t.shape
    row_width = flat.shape[1]
    step_slots = step_pairs * links

    def slot_spec(j):
        return pl.BlockSpec(
            (1, row_width, pno_width), lambda p, b: (b[p * step_slots + j], 0, 0)
        )

    grid_spec = pltpu.PrefetchScalarGridSpec(
        num_scalar_prefetch=1,
        grid=(pair_dev // step_pairs,),
        in_specs=[pl.BlockSpec((step_pairs, pno_width, pao_width), lambda p, b: (p, 0, 0))]
        + [slot_spec(j) for j in range(step_slots)],
        out_specs=pl.BlockSpec((step_pairs, pno_width, pno_width), lambda p, b: (p, 0, 0)),
    )
    flops = pair_dev * links * 2 * pno_width * pno_width * (pao_width + 2 * pno_width)
    return pl.pallas_call(
        lambda *r: linked_kernel(links, pao_width, *r),
        grid_spec=grid_spec,
        out_shape=jax.ShapeDtypeStruct((pair_dev, pno_width, pno_width), jnp.bfloat16),
        cost_estimate=pl.CostEstimate(
            flops=flops,
            bytes_accessed=pair_dev * (links * row_width + pao_width + pno_width) * pno_width * 2,
            transcendentals=0,
        ),
    )(bucket, coef_t, *([flat] * step_slots))


def local(amplitudes, pno_coef, ladder_ints, coulomb_ints, pno_energy, link_owner, link_local):
    groups = lax.axis_size("pairs")
    pair_dev = amplitudes.shape[0]
    own_rows = coulomb_ints.shape[0]
    slot_count = link_owner.shape[0]
    per_slice = slot_count // pair_dev
    capacity = max(2, (5 * slot_count + 4 * groups - 1) // (4 * groups))
    pno_width = amplitudes.shape[1]
    pao_width = pno_coef.shape[1]
    owner_group = link_owner[:, 0]
    local_index = link_local[:, 0]
    slot_order = jnp.arange(slot_count, dtype=jnp.int32)
    same_owner = (owner_group[:, None] == owner_group[None, :]) & (
        slot_order[None, :] < slot_order[:, None]
    )
    slot_rank = jnp.sum(same_owner.astype(jnp.int32), axis=1)
    bucket = owner_group * capacity + slot_rank
    places = jnp.arange(groups * capacity, dtype=jnp.int32)
    match_table = (bucket[:, None] == places[None, :]).astype(jnp.int32)
    wanted = jnp.sum(match_table * (local_index[:, None] + 1), axis=0) - 1
    asked_rows = lax.all_to_all(
        wanted.reshape(groups, capacity), "pairs", split_axis=0, concat_axis=0, tiled=True
    )
    picked = jnp.maximum(asked_rows, 0)
    both = jnp.concatenate([pno_coef, amplitudes], axis=1)
    items = both[picked.reshape(groups * capacity)]
    flat = lax.all_to_all(items, "pairs", split_axis=0, concat_axis=0, tiled=True)

    ladder_half = jnp.einsum(
        "qcd,pde->pqce", ladder_ints, amplitudes, preferred_element_type=jnp.float32
    ).astype(jnp.bfloat16)
    ladder = jnp.einsum(
        "pqce,qfe->pcf", ladder_half, ladder_ints, preferred_element_type=jnp.float32
    )
    aux_count = lax.axis_size("aux")
    aux_me = lax.axis_index("aux")
    ladder_mine = lax.dynamic_slice_in_dim(ladder, aux_me * own_rows, own_rows, 0)
    for shift in range(1, aux_count):
        goes_to = lax.rem(aux_me + shift, aux_count)
        piece = lax.dynamic_slice_in_dim(ladder, goes_to * own_rows, own_rows, 0)
        ladder_mine = ladder_mine + lax.ppermute(
            piece, "aux", [(i, (i + shift) % aux_count) for i in range(aux_count)]
        )

    flat, ladder_mine = lax.optimization_barrier((flat, ladder_mine))

    coef_t = jnp.transpose(pno_coef, (0, 2, 1))
    linked = linked_sum(bucket, coef_t, flat, per_slice)

    linked_mine = lax.dynamic_slice_in_dim(linked, aux_me * own_rows, own_rows, 0).astype(
        jnp.float32
    )
    for shift in range(1, aux_count):
        goes_to = lax.rem(aux_me + shift, aux_count)
        piece = lax.dynamic_slice_in_dim(linked, goes_to * own_rows, own_rows, 0)
        linked_mine = linked_mine + lax.ppermute(
            piece, "aux", [(i, (i + shift) % aux_count) for i in range(aux_count)]
        ).astype(jnp.float32)
    reduced = ladder_mine + linked_mine
    first_row = lax.axis_index("aux") * own_rows
    amp_mine = lax.dynamic_slice_in_dim(amplitudes, first_row, own_rows, 0)
    residual = coulomb_ints.astype(jnp.float32) + reduced
    denominator = pno_energy[:, :, None] + pno_energy[:, None, :]
    return amp_mine.astype(jnp.float32) - residual / denominator


def solution(mesh):
    in_specs = (
        P("pairs", None, None),
        P("pairs", None, None),
        P("aux", None, None),
        P(("pairs", "aux"), None, None),
        P(("pairs", "aux"), None),
        P(("pairs", "aux"), None),
        P(("pairs", "aux"), None),
    )
    out_specs = P(("pairs", "aux"), None, None)
    return jax.shard_map(local, mesh=mesh, in_specs=in_specs, out_specs=out_specs, check_vma=False)
```

```python
import jax
import jax.numpy as jnp
from jax import lax
from jax.experimental import pallas as pl
from jax.experimental.pallas import tpu as pltpu
from jax.sharding import PartitionSpec as P


def linked_kernel(links, pao_width, bucket_ref, coef_t_ref, *refs):
    slot_refs, out_ref = refs[:-1], refs[-1]
    pno_width = out_ref.shape[-1]
    for i in range(out_ref.shape[0]):
        mine = slot_refs[i * links:(i + 1) * links]
        coef_q = jnp.concatenate([r[0, :pao_width, :] for r in mine], axis=1)
        overlap = jnp.dot(coef_t_ref[i], coef_q, preferred_element_type=jnp.float32).astype(
            jnp.bfloat16
        )
        half = jnp.concatenate(
            [
                jnp.dot(
                    overlap[:, j * pno_width:(j + 1) * pno_width],
                    r[0, pao_width:, :],
                    preferred_element_type=jnp.float32,
                ).astype(jnp.bfloat16)
                for j, r in enumerate(mine)
            ],
            axis=1,
        )
        total = lax.dot_general(
            half, overlap, (((1,), (1,)), ((), ())), preferred_element_type=jnp.float32
        )
        out_ref[i] = total.astype(out_ref.dtype)


def linked_sum(bucket, coef_t, flat, links, step_pairs=4):
    pair_dev, pno_width, pao_width = coef_t.shape
    row_width = flat.shape[1]
    step_slots = step_pairs * links

    def slot_spec(j):
        return pl.BlockSpec(
            (1, row_width, pno_width), lambda p, b: (b[p * step_slots + j], 0, 0)
        )

    grid_spec = pltpu.PrefetchScalarGridSpec(
        num_scalar_prefetch=1,
        grid=(pair_dev // step_pairs,),
        in_specs=[pl.BlockSpec((step_pairs, pno_width, pao_width), lambda p, b: (p, 0, 0))]
        + [slot_spec(j) for j in range(step_slots)],
        out_specs=pl.BlockSpec((step_pairs, pno_width, pno_width), lambda p, b: (p, 0, 0)),
    )
    flops = pair_dev * links * 2 * pno_width * pno_width * (pao_width + 2 * pno_width)
    return pl.pallas_call(
        lambda *r: linked_kernel(links, pao_width, *r),
        grid_spec=grid_spec,
        out_shape=jax.ShapeDtypeStruct((pair_dev, pno_width, pno_width), jnp.bfloat16),
        cost_estimate=pl.CostEstimate(
            flops=flops,
            bytes_accessed=pair_dev * (links * row_width + pao_width + pno_width) * pno_width * 2,
            transcendentals=0,
        ),
    )(bucket, coef_t, *([flat] * step_slots))


def local(amplitudes, pno_coef, ladder_ints, coulomb_ints, pno_energy, link_owner, link_local):
    groups = lax.axis_size("pairs")
    pair_dev = amplitudes.shape[0]
    own_rows = coulomb_ints.shape[0]
    slot_count = link_owner.shape[0]
    per_slice = slot_count // pair_dev
    capacity = max(2, (5 * slot_count + 4 * groups - 1) // (4 * groups))
    pno_width = amplitudes.shape[1]
    pao_width = pno_coef.shape[1]
    owner_group = link_owner[:, 0]
    local_index = link_local[:, 0]
    slot_order = jnp.arange(slot_count, dtype=jnp.int32)
    same_owner = (owner_group[:, None] == owner_group[None, :]) & (
        slot_order[None, :] < slot_order[:, None]
    )
    slot_rank = jnp.sum(same_owner.astype(jnp.int32), axis=1)
    bucket = owner_group * capacity + slot_rank
    places = jnp.arange(groups * capacity, dtype=jnp.int32)
    match_table = (bucket[:, None] == places[None, :]).astype(jnp.int32)
    wanted = jnp.sum(match_table * (local_index[:, None] + 1), axis=0) - 1
    asked_rows = lax.all_to_all(
        wanted.reshape(groups, capacity), "pairs", split_axis=0, concat_axis=0, tiled=True
    )
    def ladder_of(amps):
        ladder_half = jnp.einsum(
            "qcd,pde->pqce", ladder_ints, amps, preferred_element_type=jnp.float32
        ).astype(jnp.bfloat16)
        return jnp.einsum(
            "pqce,qfe->pcf", ladder_half, ladder_ints, preferred_element_type=jnp.float32
        )

    split = pair_dev // 2
    ladder_first = ladder_of(amplitudes[:split])
    picked = jnp.maximum(asked_rows, 0)
    picked, ladder_first = lax.optimization_barrier((picked, ladder_first))
    both = jnp.concatenate([pno_coef, amplitudes], axis=1)
    items = both[picked.reshape(groups * capacity)]
    flat = lax.all_to_all(items, "pairs", split_axis=0, concat_axis=0, tiled=True)

    ladder = jnp.concatenate([ladder_first, ladder_of(amplitudes[split:])], axis=0)

    aux_count = lax.axis_size("aux")
    aux_me = lax.axis_index("aux")
    ladder_mine = lax.dynamic_slice_in_dim(ladder, aux_me * own_rows, own_rows, 0)
    for shift in range(1, aux_count):
        goes_to = lax.rem(aux_me + shift, aux_count)
        piece = lax.dynamic_slice_in_dim(ladder, goes_to * own_rows, own_rows, 0)
        ladder_mine = ladder_mine + lax.ppermute(
            piece, "aux", [(i, (i + shift) % aux_count) for i in range(aux_count)]
        )

    flat, ladder_mine = lax.optimization_barrier((flat, ladder_mine))

    coef_t = jnp.transpose(pno_coef, (0, 2, 1))
    linked = linked_sum(bucket, coef_t, flat, per_slice)

    pieces = linked.reshape(aux_count, own_rows, pno_width, pno_width)
    linked_mine = jnp.sum(
        lax.all_to_all(pieces, "aux", split_axis=0, concat_axis=0, tiled=True).astype(jnp.float32),
        axis=0,
    )
    reduced = ladder_mine + linked_mine
    first_row = lax.axis_index("aux") * own_rows
    amp_mine = lax.dynamic_slice_in_dim(amplitudes, first_row, own_rows, 0)
    residual = coulomb_ints.astype(jnp.float32) + reduced
    denominator = pno_energy[:, :, None] + pno_energy[:, None, :]
    return amp_mine.astype(jnp.float32) - residual / denominator


def solution(mesh):
    in_specs = (
        P("pairs", None, None),
        P("pairs", None, None),
        P("aux", None, None),
        P(("pairs", "aux"), None, None),
        P(("pairs", "aux"), None),
        P(("pairs", "aux"), None),
        P(("pairs", "aux"), None),
    )
    out_specs = P(("pairs", "aux"), None, None)
    return jax.shard_map(local, mesh=mesh, in_specs=in_specs, out_specs=out_specs, check_vma=False)
```

```python
import jax
import jax.numpy as jnp
from jax import lax
from jax.experimental import pallas as pl
from jax.experimental.pallas import tpu as pltpu
from jax.sharding import PartitionSpec as P


def linked_kernel(links, pao_width, bucket_ref, coef_t_ref, *refs):
    slot_refs, out_ref = refs[:-1], refs[-1]
    pno_width = out_ref.shape[-1]
    for i in range(out_ref.shape[0]):
        mine = slot_refs[i * links:(i + 1) * links]
        coef_q = jnp.concatenate([r[0, :pao_width, :] for r in mine], axis=1)
        overlap = jnp.dot(coef_t_ref[i], coef_q, preferred_element_type=jnp.float32).astype(
            jnp.bfloat16
        )
        half = jnp.concatenate(
            [
                jnp.dot(
                    overlap[:, j * pno_width:(j + 1) * pno_width],
                    r[0, pao_width:, :],
                    preferred_element_type=jnp.float32,
                ).astype(jnp.bfloat16)
                for j, r in enumerate(mine)
            ],
            axis=1,
        )
        total = lax.dot_general(
            half, overlap, (((1,), (1,)), ((), ())), preferred_element_type=jnp.float32
        )
        out_ref[i] = total.astype(out_ref.dtype)


def linked_sum(bucket, coef_t, flat, links, step_pairs=4):
    pair_dev, pno_width, pao_width = coef_t.shape
    row_width = flat.shape[1]
    step_slots = step_pairs * links

    def slot_spec(j):
        return pl.BlockSpec(
            (1, row_width, pno_width), lambda p, b: (b[p * step_slots + j], 0, 0)
        )

    grid_spec = pltpu.PrefetchScalarGridSpec(
        num_scalar_prefetch=1,
        grid=(pair_dev // step_pairs,),
        in_specs=[pl.BlockSpec((step_pairs, pno_width, pao_width), lambda p, b: (p, 0, 0))]
        + [slot_spec(j) for j in range(step_slots)],
        out_specs=pl.BlockSpec((step_pairs, pno_width, pno_width), lambda p, b: (p, 0, 0)),
    )
    flops = pair_dev * links * 2 * pno_width * pno_width * (pao_width + 2 * pno_width)
    return pl.pallas_call(
        lambda *r: linked_kernel(links, pao_width, *r),
        grid_spec=grid_spec,
        out_shape=jax.ShapeDtypeStruct((pair_dev, pno_width, pno_width), jnp.bfloat16),
        cost_estimate=pl.CostEstimate(
            flops=flops,
            bytes_accessed=pair_dev * (links * row_width + pao_width + pno_width) * pno_width * 2,
            transcendentals=0,
        ),
    )(bucket, coef_t, *([flat] * step_slots))


def local(amplitudes, pno_coef, ladder_ints, coulomb_ints, pno_energy, link_owner, link_local):
    groups = lax.axis_size("pairs")
    pair_dev = amplitudes.shape[0]
    own_rows = coulomb_ints.shape[0]
    slot_count = link_owner.shape[0]
    per_slice = slot_count // pair_dev
    capacity = max(2, (5 * slot_count + 4 * groups - 1) // (4 * groups))
    pno_width = amplitudes.shape[1]
    pao_width = pno_coef.shape[1]
    owner_group = link_owner[:, 0]
    local_index = link_local[:, 0]
    slot_order = jnp.arange(slot_count, dtype=jnp.int32)
    same_owner = (owner_group[:, None] == owner_group[None, :]) & (
        slot_order[None, :] < slot_order[:, None]
    )
    slot_rank = jnp.sum(same_owner.astype(jnp.int32), axis=1)
    bucket = owner_group * capacity + slot_rank
    places = jnp.arange(groups * capacity, dtype=jnp.int32)
    match_table = (bucket[:, None] == places[None, :]).astype(jnp.int32)
    wanted = jnp.sum(match_table * (local_index[:, None] + 1), axis=0) - 1
    asked_rows = lax.all_to_all(
        wanted.reshape(groups, capacity), "pairs", split_axis=0, concat_axis=0, tiled=True
    )
    picked = jnp.maximum(asked_rows, 0)
    both = jnp.concatenate([pno_coef, amplitudes], axis=1)
    items = both[picked.reshape(groups * capacity)]
    flat = lax.all_to_all(items, "pairs", split_axis=0, concat_axis=0, tiled=True)

    ladder_half = jnp.einsum(
        "qcd,pde->pqce", ladder_ints, amplitudes, preferred_element_type=jnp.float32
    ).astype(jnp.bfloat16)
    ladder = jnp.einsum(
        "pqce,qfe->pcf", ladder_half, ladder_ints, preferred_element_type=jnp.float32
    )
    aux_count = lax.axis_size("aux")
    aux_me = lax.axis_index("aux")
    ladder_mine = lax.dynamic_slice_in_dim(ladder, aux_me * own_rows, own_rows, 0)
    for shift in range(1, aux_count):
        goes_to = lax.rem(aux_me + shift, aux_count)
        piece = lax.dynamic_slice_in_dim(ladder, goes_to * own_rows, own_rows, 0)
        ladder_mine = ladder_mine + lax.ppermute(
            piece, "aux", [(i, (i + shift) % aux_count) for i in range(aux_count)]
        )

    flat, ladder_mine = lax.optimization_barrier((flat, ladder_mine))

    coef_t = jnp.transpose(pno_coef, (0, 2, 1))
    bucket_rows = bucket.reshape(pair_dev, per_slice)
    sums = []
    for parity in range(own_rows):
        linked = linked_sum(
            bucket_rows[parity::own_rows].reshape(-1), coef_t[parity::own_rows], flat, per_slice
        )
        pieces = linked.reshape(aux_count, 1, pno_width, pno_width)
        sums.append(
            jnp.sum(
                lax.all_to_all(pieces, "aux", split_axis=0, concat_axis=0, tiled=True).astype(
                    jnp.float32
                ),
                axis=0,
            )
        )
    linked_mine = jnp.concatenate(sums, axis=0)
    reduced = ladder_mine + linked_mine
    first_row = lax.axis_index("aux") * own_rows
    amp_mine = lax.dynamic_slice_in_dim(amplitudes, first_row, own_rows, 0)
    residual = coulomb_ints.astype(jnp.float32) + reduced
    denominator = pno_energy[:, :, None] + pno_energy[:, None, :]
    return amp_mine.astype(jnp.float32) - residual / denominator


def solution(mesh):
    in_specs = (
        P("pairs", None, None),
        P("pairs", None, None),
        P("aux", None, None),
        P(("pairs", "aux"), None, None),
        P(("pairs", "aux"), None),
        P(("pairs", "aux"), None),
        P(("pairs", "aux"), None),
    )
    out_specs = P(("pairs", "aux"), None, None)
    return jax.shard_map(local, mesh=mesh, in_specs=in_specs, out_specs=out_specs, check_vma=False)
```

```python
import jax
import jax.numpy as jnp
from jax import lax
from jax.experimental import pallas as pl
from jax.experimental.pallas import tpu as pltpu
from jax.sharding import PartitionSpec as P


def linked_kernel(links, pao_width, bucket_ref, coef_t_ref, *refs):
    slot_refs, out_ref = refs[:-1], refs[-1]
    pno_width = out_ref.shape[-1]
    for i in range(out_ref.shape[0]):
        mine = slot_refs[i * links:(i + 1) * links]
        coef_q = jnp.concatenate([r[0, :pao_width, :] for r in mine], axis=1)
        overlap = jnp.dot(coef_t_ref[i], coef_q, preferred_element_type=jnp.float32).astype(
            jnp.bfloat16
        )
        half = jnp.concatenate(
            [
                jnp.dot(
                    overlap[:, j * pno_width:(j + 1) * pno_width],
                    r[0, pao_width:, :],
                    preferred_element_type=jnp.float32,
                ).astype(jnp.bfloat16)
                for j, r in enumerate(mine)
            ],
            axis=1,
        )
        total = lax.dot_general(
            half, overlap, (((1,), (1,)), ((), ())), preferred_element_type=jnp.float32
        )
        out_ref[i] = total.astype(out_ref.dtype)


def linked_sum(bucket, coef_t, flat, links, step_pairs=4):
    pair_dev, pno_width, pao_width = coef_t.shape
    row_width = flat.shape[1]
    step_slots = step_pairs * links

    def slot_spec(j):
        return pl.BlockSpec(
            (1, row_width, pno_width), lambda p, b: (b[p * step_slots + j], 0, 0)
        )

    grid_spec = pltpu.PrefetchScalarGridSpec(
        num_scalar_prefetch=1,
        grid=(pair_dev // step_pairs,),
        in_specs=[pl.BlockSpec((step_pairs, pno_width, pao_width), lambda p, b: (p, 0, 0))]
        + [slot_spec(j) for j in range(step_slots)],
        out_specs=pl.BlockSpec((step_pairs, pno_width, pno_width), lambda p, b: (p, 0, 0)),
    )
    flops = pair_dev * links * 2 * pno_width * pno_width * (pao_width + 2 * pno_width)
    return pl.pallas_call(
        lambda *r: linked_kernel(links, pao_width, *r),
        grid_spec=grid_spec,
        out_shape=jax.ShapeDtypeStruct((pair_dev, pno_width, pno_width), jnp.bfloat16),
        cost_estimate=pl.CostEstimate(
            flops=flops,
            bytes_accessed=pair_dev * (links * row_width + pao_width + pno_width) * pno_width * 2,
            transcendentals=0,
        ),
    )(bucket, coef_t, *([flat] * step_slots))


def local(amplitudes, pno_coef, ladder_ints, coulomb_ints, pno_energy, link_owner, link_local):
    groups = lax.axis_size("pairs")
    pair_dev = amplitudes.shape[0]
    own_rows = coulomb_ints.shape[0]
    slot_count = link_owner.shape[0]
    per_slice = slot_count // pair_dev
    capacity = max(2, (5 * slot_count + 4 * groups - 1) // (4 * groups))
    pno_width = amplitudes.shape[1]
    pao_width = pno_coef.shape[1]
    owner_group = link_owner[:, 0]
    local_index = link_local[:, 0]
    slot_order = jnp.arange(slot_count, dtype=jnp.int32)
    same_owner = (owner_group[:, None] == owner_group[None, :]) & (
        slot_order[None, :] < slot_order[:, None]
    )
    slot_rank = jnp.sum(same_owner.astype(jnp.int32), axis=1)
    bucket = owner_group * capacity + slot_rank
    places = jnp.arange(groups * capacity, dtype=jnp.int32)
    match_table = (bucket[:, None] == places[None, :]).astype(jnp.int32)
    wanted = jnp.sum(match_table * (local_index[:, None] + 1), axis=0) - 1
    asked_rows = lax.all_to_all(
        wanted.reshape(groups, capacity), "pairs", split_axis=0, concat_axis=0, tiled=True
    )
    picked = jnp.maximum(asked_rows, 0)
    both = jnp.concatenate([pno_coef, amplitudes], axis=1)
    items = both[picked.reshape(groups * capacity)]
    flat = lax.all_to_all(items, "pairs", split_axis=0, concat_axis=0, tiled=True)

    ladder_half = jnp.einsum(
        "qcd,pde->pqce", ladder_ints, amplitudes, preferred_element_type=jnp.float32
    ).astype(jnp.bfloat16)
    ladder = jnp.einsum(
        "pqce,qfe->pcf", ladder_half, ladder_ints, preferred_element_type=jnp.float32
    )
    aux_count = lax.axis_size("aux")
    aux_me = lax.axis_index("aux")
    ladder_mine = lax.dynamic_slice_in_dim(ladder, aux_me * own_rows, own_rows, 0)
    for shift in range(1, aux_count):
        goes_to = lax.rem(aux_me + shift, aux_count)
        piece = lax.dynamic_slice_in_dim(ladder, goes_to * own_rows, own_rows, 0)
        ladder_mine = ladder_mine + lax.ppermute(
            piece, "aux", [(i, (i + shift) % aux_count) for i in range(aux_count)]
        )

    amp_mine = lax.dynamic_slice_in_dim(amplitudes, aux_me * own_rows, own_rows, 0)
    denominator = pno_energy[:, :, None] + pno_energy[:, None, :]
    base = amp_mine.astype(jnp.float32) - (
        coulomb_ints.astype(jnp.float32) + ladder_mine
    ) / denominator
    flat, base = lax.optimization_barrier((flat, base))

    coef_t = jnp.transpose(pno_coef, (0, 2, 1))
    linked = linked_sum(bucket, coef_t, flat, per_slice)

    pieces = linked.reshape(aux_count, own_rows, pno_width, pno_width)
    linked_mine = jnp.sum(
        lax.all_to_all(pieces, "aux", split_axis=0, concat_axis=0, tiled=True).astype(jnp.float32),
        axis=0,
    )
    return base - linked_mine / denominator


def solution(mesh):
    in_specs = (
        P("pairs", None, None),
        P("pairs", None, None),
        P("aux", None, None),
        P(("pairs", "aux"), None, None),
        P(("pairs", "aux"), None),
        P(("pairs", "aux"), None),
        P(("pairs", "aux"), None),
    )
    out_specs = P(("pairs", "aux"), None, None)
    return jax.shard_map(local, mesh=mesh, in_specs=in_specs, out_specs=out_specs, check_vma=False)
```

```python
import jax
import jax.numpy as jnp
from jax import lax
from jax.experimental import pallas as pl
from jax.experimental.pallas import tpu as pltpu
from jax.sharding import PartitionSpec as P


def linked_kernel(links, pao_width, bucket_ref, coef_t_ref, *refs):
    slot_refs, out_ref = refs[:-1], refs[-1]
    pno_width = out_ref.shape[-1]
    for i in range(out_ref.shape[0]):
        mine = slot_refs[i * links:(i + 1) * links]
        coef_q = jnp.concatenate([r[0, :pao_width, :] for r in mine], axis=1)
        overlap = jnp.dot(coef_t_ref[i], coef_q, preferred_element_type=jnp.float32).astype(
            jnp.bfloat16
        )
        half = jnp.concatenate(
            [
                jnp.dot(
                    overlap[:, j * pno_width:(j + 1) * pno_width],
                    r[0, pao_width:, :],
                    preferred_element_type=jnp.float32,
                ).astype(jnp.bfloat16)
                for j, r in enumerate(mine)
            ],
            axis=1,
        )
        total = lax.dot_general(
            half, overlap, (((1,), (1,)), ((), ())), preferred_element_type=jnp.float32
        )
        out_ref[i] = total.astype(out_ref.dtype)


def linked_sum(bucket, coef_t, flat, links, step_pairs=4):
    pair_dev, pno_width, pao_width = coef_t.shape
    row_width = flat.shape[1]
    step_slots = step_pairs * links

    def slot_spec(j):
        return pl.BlockSpec(
            (1, row_width, pno_width), lambda p, b: (b[p * step_slots + j], 0, 0)
        )

    grid_spec = pltpu.PrefetchScalarGridSpec(
        num_scalar_prefetch=1,
        grid=(pair_dev // step_pairs,),
        in_specs=[pl.BlockSpec((step_pairs, pno_width, pao_width), lambda p, b: (p, 0, 0))]
        + [slot_spec(j) for j in range(step_slots)],
        out_specs=pl.BlockSpec((step_pairs, pno_width, pno_width), lambda p, b: (p, 0, 0)),
    )
    flops = pair_dev * links * 2 * pno_width * pno_width * (pao_width + 2 * pno_width)
    return pl.pallas_call(
        lambda *r: linked_kernel(links, pao_width, *r),
        grid_spec=grid_spec,
        out_shape=jax.ShapeDtypeStruct((pair_dev, pno_width, pno_width), jnp.bfloat16),
        cost_estimate=pl.CostEstimate(
            flops=flops,
            bytes_accessed=pair_dev * (links * row_width + pao_width + pno_width) * pno_width * 2,
            transcendentals=0,
        ),
    )(bucket, coef_t, *([flat] * step_slots))


def local(amplitudes, pno_coef, ladder_ints, coulomb_ints, pno_energy, link_owner, link_local):
    groups = lax.axis_size("pairs")
    pair_dev = amplitudes.shape[0]
    own_rows = coulomb_ints.shape[0]
    slot_count = link_owner.shape[0]
    per_slice = slot_count // pair_dev
    capacity = max(2, (5 * slot_count + 4 * groups - 1) // (4 * groups))
    pno_width = amplitudes.shape[1]
    pao_width = pno_coef.shape[1]
    owner_group = link_owner[:, 0]
    local_index = link_local[:, 0]
    slot_order = jnp.arange(slot_count, dtype=jnp.int32)
    same_owner = (owner_group[:, None] == owner_group[None, :]) & (
        slot_order[None, :] < slot_order[:, None]
    )
    slot_rank = jnp.sum(same_owner.astype(jnp.int32), axis=1)
    bucket = owner_group * capacity + slot_rank
    places = jnp.arange(groups * capacity, dtype=jnp.int32)
    match_table = (bucket[:, None] == places[None, :]).astype(jnp.int32)
    wanted = jnp.sum(match_table * (local_index[:, None] + 1), axis=0) - 1
    asked_rows = lax.all_to_all(
        wanted.reshape(groups, capacity), "pairs", split_axis=0, concat_axis=0, tiled=True
    )
    picked = jnp.maximum(asked_rows, 0)
    both = jnp.concatenate([pno_coef, amplitudes], axis=1)
    items = both[picked.reshape(groups * capacity)]
    flat = lax.all_to_all(items, "pairs", split_axis=0, concat_axis=0, tiled=True)

    ladder_half = jnp.einsum(
        "qcd,pde->pqce", ladder_ints, amplitudes, preferred_element_type=jnp.float32
    ).astype(jnp.bfloat16)
    ladder = jnp.einsum(
        "pqce,qfe->pcf", ladder_half, ladder_ints, preferred_element_type=jnp.float32
    )
    aux_count = lax.axis_size("aux")
    aux_me = lax.axis_index("aux")
    ladder_mine = lax.dynamic_slice_in_dim(ladder, aux_me * own_rows, own_rows, 0)
    for shift in range(1, aux_count):
        goes_to = lax.rem(aux_me + shift, aux_count)
        piece = lax.dynamic_slice_in_dim(ladder, goes_to * own_rows, own_rows, 0)
        ladder_mine = ladder_mine + lax.ppermute(
            piece, "aux", [(i, (i + shift) % aux_count) for i in range(aux_count)]
        )

    amp_mine = lax.dynamic_slice_in_dim(amplitudes, aux_me * own_rows, own_rows, 0)
    denominator = pno_energy[:, :, None] + pno_energy[:, None, :]
    base = amp_mine.astype(jnp.float32) - (
        coulomb_ints.astype(jnp.float32) + ladder_mine
    ) / denominator
    flat, base = lax.optimization_barrier((flat, base))

    coef_t = jnp.transpose(pno_coef, (0, 2, 1))
    linked = linked_sum(bucket, coef_t, flat, per_slice)

    pieces = linked.reshape(aux_count, own_rows, pno_width, pno_width)
    got = lax.all_to_all(pieces, "aux", split_axis=0, concat_axis=0, tiled=True)
    linked_mine = got[0].astype(jnp.float32)
    for source in range(1, aux_count):
        linked_mine = linked_mine + got[source].astype(jnp.float32)
    return base - linked_mine / denominator


def solution(mesh):
    in_specs = (
        P("pairs", None, None),
        P("pairs", None, None),
        P("aux", None, None),
        P(("pairs", "aux"), None, None),
        P(("pairs", "aux"), None),
        P(("pairs", "aux"), None),
        P(("pairs", "aux"), None),
    )
    out_specs = P(("pairs", "aux"), None, None)
    return jax.shard_map(local, mesh=mesh, in_specs=in_specs, out_specs=out_specs, check_vma=False)
```
